128 devices in a mesh: row: 4 (over z_hi, core), circ: 32 (over x, y, z_lo).
Axes of the slice: x: 4, y: 4, z: 4 (z_hi: 2, z_lo: 2; z = z_hi * 2 + z_lo), core: 2. Of those that a mesh axis runs over, the one named last changes fastest.
Arguments:
- flow_state: float32 [5, 64, 32, 4096], P(None, 'row', None, 'circ'), may hold values from -4 to 4
- velocity: float32 [3, 64, 32, 4096], P(None, 'row', None, 'circ'), may hold values from -3 to 3
- offsets: int32 [3, 3], replicated, may hold values from 0 to 4095, as said below
- passage_shift: int32 [4], replicated, may hold values from 0 to 31, as said below
- donor_step: int32 [4, 2, 4096], P('row', None, 'circ'), may hold values from 0 to 127
- donor_weight: float32 [4, 2, 4096], P('row', None, 'circ'), may hold values from 0.05 to 0.95
Outputs:
- updated_state: float32 [5, 64, 32, 4096], P(None, 'row', None, 'circ')
The draws below stay inside these ranges and needn't reach their ends.
Inputs may be any that keep to these rules, and one draw needn't show every extreme that they name: Rotation offsets in cells; some interface takes the offset 4096 - 1 at some section in every draw, and with two or more interfaces some takes 0. `passage_shift`: passage index placed on device column 0 of each row; some row has 32 - 1 and some row 0 in every draw.
All inputs are finite; a program needn't handle non-finite values.
Results may differ from the reference program's by a relative error of at most 0.0003.
Values sent between devices are 32-bit elements; how exact they have to be, the bound alone decides.
No kernel may reach another device: no remote copies, remote signals or barrier semaphores. Data moves between devices by JAX's collectives and lax.ppermute only.
A program may use at most 128 MiB of HBM per device.

```python
import jax
import jax.numpy as jnp
from jax import lax

AX = 16
RA = 32
CC = 128
SECTIONS = 3
COMPS = 5
ROWS = 4
IFACES = 3
PASSAGES = 32
AXIAL = 64
NC = 4096


def joint_draw(key):
    base = jax.random.fold_in(key, 4711)
    key_shift = jax.random.fold_in(base, 1)
    key_offs = jax.random.fold_in(base, 2)
    key_part = jax.random.fold_in(base, 3)
    key_near = jax.random.fold_in(base, 5)
    shifts = jax.random.randint(key_shift, (ROWS,), 0, PASSAGES, dtype=jnp.int32)
    row_ids = jnp.arange(ROWS, dtype=jnp.int32)
    shifts = jnp.where(row_ids == 0, PASSAGES - 1, shifts)
    shifts = jnp.where(row_ids == ROWS - 1, 0, shifts)
    offs = jax.random.randint(key_offs, (SECTIONS, IFACES), 0, NC, dtype=jnp.int32)
    within = jax.random.randint(key_part, (IFACES,), 0, CC, dtype=jnp.int32)
    near_within = jax.random.randint(key_near, (IFACES,), 0, CC, dtype=jnp.int32)
    forced = (PASSAGES // 2 - shifts[:-1] + shifts[1:]) % PASSAGES * CC + within
    behind = (shifts[1:] - shifts[:-1] - 1) % PASSAGES * CC + near_within
    section_row = jnp.arange(SECTIONS, dtype=jnp.int32)[:, None]
    face_col = jnp.arange(IFACES, dtype=jnp.int32)[None, :]
    offs = jnp.where(section_row == 0, forced[None, :], offs)
    offs = jnp.where(section_row == 1, behind[None, :], offs)
    offs = jnp.where((section_row == 2) & (face_col == 0), NC - 1, offs)
    if IFACES > 1:
        offs = jnp.where((section_row == 2) & (face_col == IFACES - 1), 0, offs)
    return (shifts, offs)


def draw_offsets(key, part):
    return joint_draw(key)[1]


def draw_passage_shift(key, part):
    return joint_draw(key)[0]


def place_ends(entries, rng, low, largest):
    index_at = [jax.random.randint(jax.random.fold_in(rng, axis), (), 0, length) for axis, length in enumerate(entries.shape)]
    longest = entries.shape.index(max(entries.shape))
    neighbour = index_at[:longest] + [(index_at[longest] + 1) % entries.shape[longest]] + index_at[longest + 1:]
    return entries.at[tuple(index_at)].set(low).at[tuple(neighbour)].set(largest)


def block_levels(own_key, extent, pieces, low, high):
    loudness = 1.0
    for dim, parts in pieces:
        draws = jax.random.uniform(jax.random.fold_in(jax.random.fold_in(own_key, 6), dim), (parts,), jnp.float32, low / len(pieces), high / len(pieces))
        loudness = loudness * jnp.repeat(jnp.exp(draws), extent[dim] // parts).reshape((-1,) + (1,) * (len(extent) - 1 - dim))
    return loudness


def noise(rng, shape, scale, bound, cuts=(), kind=jnp.bfloat16):
    loudness = block_levels(rng, shape, cuts, -0.22, 0.18) if cuts else 1.0
    values = jax.random.normal(rng, shape, jnp.float32) * scale * loudness
    return jnp.minimum(jnp.maximum(values, -bound), bound).astype(kind)


def setup_inputs(seed: int = 0) -> dict:
    seeds = jax.random.split(jax.random.key(seed), 7)
    return {
        "flow_state": noise(seeds[0], (COMPS, AXIAL, RA, NC), 1.0, 4.0, ((1, 4), (3, 32)), jnp.float32),
        "velocity": noise(seeds[1], (3, AXIAL, RA, NC), 0.6, 3.0, ((1, 4), (3, 32)), jnp.float32),
        "offsets": draw_offsets(jax.random.fold_in(seeds[6], 71), 0),
        "passage_shift": draw_passage_shift(jax.random.fold_in(seeds[6], 71), 0),
        "donor_step": place_ends(jax.random.randint(seeds[4], (ROWS, 2, NC), 0, CC), jax.random.fold_in(seeds[4], 1), 0, CC - 1).astype(jnp.int32),
        "donor_weight": jnp.clip(0.05 + 0.9 * jax.random.uniform(seeds[5], (ROWS, 2, NC), jnp.float32) ** block_levels(seeds[5], (ROWS, 2, NC), ((0, 4), (2, 32)), -0.2, 0.2), 0.05, 0.95),
    }


SMAG_COEF = 0.1
TIME_STEP = 0.25

def combine(fields, axial_ext, radial_ext, around_ext, velocity):
    d_axial = 0.5 * (axial_ext[:, 2:] - axial_ext[:, :-2])
    d_radial = 0.5 * (radial_ext[:, :, 2:] - radial_ext[:, :, :-2])
    d_around = 0.5 * (around_ext[..., 2:] - around_ext[..., :-2])
    laplace = axial_ext[:, 2:] + axial_ext[:, :-2] + radial_ext[:, :, 2:] + radial_ext[:, :, :-2] + around_ext[..., 2:] + around_ext[..., :-2] - 6.0 * fields
    strain = lax.optimization_barrier(jnp.sum(d_axial[1:4] ** 2 + d_radial[1:4] ** 2 + d_around[1:4] ** 2, axis=0))
    eddy_visc = SMAG_COEF * jnp.sqrt(strain + 1.0)
    return eddy_visc * laplace - (velocity[0] * d_axial + velocity[1] * d_radial + velocity[2] * d_around)

def radial_pad(fields):
    return jnp.concatenate([fields[:, :, :1], fields, fields[:, :, -1:]], axis=2)

def axial_pad(fields, lower_ghost, upper_ghost):
    return jnp.concatenate([lower_ghost[:, None], fields, upper_ghost[:, None]], axis=1)

def ghost_plane(source, donor_steps, weights, offset, loop_cells):
    donor_cols = (jnp.arange(loop_cells, dtype=jnp.int32) + offset + donor_steps) % loop_cells
    next_cols = (donor_cols + 1) % loop_cells
    return weights * source[:, :, donor_cols] + (1.0 - weights) * source[:, :, next_cols]

def reference(flow_state, velocity, offsets, passage_shift, donor_step, donor_weight):
    loop_cells = flow_state.shape[-1]

    def ordered(values, row_index):
        return jnp.roll(values, -passage_shift[row_index] * CC, axis=-1)
    start_rows = [ordered(flow_state[:, row_index * AX:(row_index + 1) * AX], row_index) for row_index in range(ROWS)]
    speeds = [ordered(velocity[:, row_index * AX:(row_index + 1) * AX], row_index) for row_index in range(ROWS)]
    donor_cols = [ordered(donor_step[row_index], row_index) for row_index in range(ROWS)]
    donor_wts = [ordered(donor_weight[row_index], row_index) for row_index in range(ROWS)]

    def evaluate(fields_list, section_index):
        result = []
        for row_index in range(ROWS):
            fields = fields_list[row_index]
            if row_index > 0:
                lower_ghost = ghost_plane(fields_list[row_index - 1][:, -1], donor_cols[row_index][0], donor_wts[row_index][0], offsets[section_index, row_index - 1], loop_cells)
            else:
                lower_ghost = fields[:, 0]
            if row_index < ROWS - 1:
                upper_ghost = ghost_plane(fields_list[row_index + 1][:, 0], donor_cols[row_index][1], donor_wts[row_index][1], -offsets[section_index, row_index], loop_cells)
            else:
                upper_ghost = fields[:, -1]
            around_ext = jnp.concatenate([fields[..., -1:], fields, fields[..., :1]], axis=3)
            result.append(combine(fields, axial_pad(fields, lower_ghost, upper_ghost), radial_pad(fields), around_ext, speeds[row_index]))
        return result
    first_rate = evaluate(start_rows, 0)
    section_one = [start_rows[row_index] + TIME_STEP * first_rate[row_index] for row_index in range(ROWS)]
    second_rate = evaluate(section_one, 1)
    section_two = [0.75 * start_rows[row_index] + 0.25 * (section_one[row_index] + TIME_STEP * second_rate[row_index]) for row_index in range(ROWS)]
    third_rate = evaluate(section_two, 2)
    section_three = [1.0 / 3.0 * start_rows[row_index] + 2.0 / 3.0 * (section_two[row_index] + TIME_STEP * third_rate[row_index]) for row_index in range(ROWS)]
    restored = [jnp.roll(section_three[row_index], passage_shift[row_index] * CC, axis=-1) for row_index in range(ROWS)]
    return jnp.concatenate(restored, axis=1)
```

```python
import jax
import jax.numpy as jnp
from jax import lax
from jax.sharding import PartitionSpec as P

SMAG_COEF = 0.1
TIME_STEP = 0.25
RADICES = (8, 4)


def extended(cells, sides, width):
    for axis, dim in sides:
        count = lax.axis_size(axis)
        head = lax.slice_in_dim(cells, 0, width, axis=dim)
        tail = lax.slice_in_dim(cells, cells.shape[dim] - width, cells.shape[dim], axis=dim)
        cells = jnp.concatenate(
            [
                lax.ppermute(tail, axis, [(i, (i + 1) % count) for i in range(count)]),
                cells,
                lax.ppermute(head, axis, [((i + 1) % count, i) for i in range(count)]),
            ],
            axis=dim,
        )
    return cells


def combine(fields, axial_ext, radial_ext, around_ext, velocity):
    d_axial = 0.5 * (axial_ext[:, 2:] - axial_ext[:, :-2])
    d_radial = 0.5 * (radial_ext[:, :, 2:] - radial_ext[:, :, :-2])
    d_around = 0.5 * (around_ext[..., 2:] - around_ext[..., :-2])
    laplace = (
        axial_ext[:, 2:]
        + axial_ext[:, :-2]
        + radial_ext[:, :, 2:]
        + radial_ext[:, :, :-2]
        + around_ext[..., 2:]
        + around_ext[..., :-2]
        - 6.0 * fields
    )
    strain = jnp.sum(d_axial[1:4] ** 2 + d_radial[1:4] ** 2 + d_around[1:4] ** 2, axis=0)
    eddy_visc = SMAG_COEF * jnp.sqrt(strain + 1.0)
    return eddy_visc * laplace - (
        velocity[0] * d_axial + velocity[1] * d_radial + velocity[2] * d_around
    )


def radial_pad(fields):
    return jnp.concatenate([fields[:, :, :1], fields, fields[:, :, -1:]], axis=2)


def axial_pad(fields, lower_ghost, upper_ghost):
    return jnp.concatenate([lower_ghost[:, None], fields, upper_ghost[:, None]], axis=1)


def local(flow_state, velocity, offsets, passage_shift, donor_step, donor_weight):
    row_count = lax.axis_size("row")
    loop_size = lax.axis_size("circ")
    row_id = lax.axis_index("row")
    pitch_cells = flow_state.shape[-1]
    loop_cells = pitch_cells * loop_size
    lower_src = jnp.maximum(row_id - 1, 0)
    upper_src = jnp.minimum(row_id + 1, row_count - 1)
    lower_face = jnp.maximum(row_id - 1, 0)
    upper_face = jnp.minimum(row_id, row_count - 2)
    window = 3 * pitch_cells

    def from_row(plane, step, shift):
        pairs = []
        for r in range(row_count):
            src = r + step
            if 0 <= src < row_count:
                for b in range(loop_size):
                    pairs.append((src * loop_size + (b + shift) % loop_size, r * loop_size + b))
        return lax.ppermute(plane, ("row", "circ"), pairs)

    def along_circ(value, shift):
        return lax.ppermute(
            value, "circ", [((b + shift) % loop_size, b) for b in range(loop_size)]
        )

    def blocks_of(plane, step, dq):
        first = RADICES[0]
        got = [from_row(plane, step, j) for j in range(first + 2)]
        digit = dq % first
        stack = jnp.stack([lax.select_n(digit, *got[i : i + first]) for i in range(3)])
        span = first
        rest = dq // first
        for radix in RADICES[1:]:
            digit = rest % radix
            rest = rest // radix
            got = [stack] + [along_circ(stack, span * c) for c in range(1, radix)]
            stack = lax.select_n(digit, *got)
            span *= radix
        return stack

    def interface(plane, step, source_row, offset, donor_steps, weights):
        coarse = offset // pitch_cells
        fine = offset % pitch_cells
        dq = (coarse + passage_shift[source_row] - passage_shift[row_id]) % loop_size
        stack = blocks_of(plane, step, dq)
        comps, radial = plane.shape[0], plane.shape[1]
        win = jnp.transpose(stack, (1, 2, 0, 3)).reshape(comps * radial, window)
        first_col = jnp.arange(pitch_cells, dtype=jnp.int32) + fine + donor_steps
        rows = jnp.arange(window, dtype=jnp.int32)[:, None]
        pick = jnp.where(rows == first_col[None, :], weights[None, :], 0.0) + jnp.where(
            rows == first_col[None, :] + 1, 1.0 - weights[None, :], 0.0
        )
        ghost = jnp.dot(win, pick, precision=lax.Precision.HIGHEST)
        return ghost.reshape(comps, radial, pitch_cells)

    def evaluate(fields, section_index):
        first_plane = fields[:, 0]
        last_plane = fields[:, -1]
        low_offset = offsets[section_index, lower_face]
        high_offset = (loop_cells - offsets[section_index, upper_face]) % loop_cells
        lower_ghost = interface(
            last_plane, -1, lower_src, low_offset, donor_step[0, 0], donor_weight[0, 0]
        )
        upper_ghost = interface(
            first_plane, 1, upper_src, high_offset, donor_step[0, 1], donor_weight[0, 1]
        )
        lower_ghost = jnp.where(row_id == 0, first_plane, lower_ghost)
        upper_ghost = jnp.where(row_id == row_count - 1, last_plane, upper_ghost)
        around_ext = extended(fields, (("circ", 3),), 1)
        return combine(
            fields,
            axial_pad(fields, lower_ghost, upper_ghost),
            radial_pad(fields),
            around_ext,
            velocity,
        )

    section_one = flow_state + TIME_STEP * evaluate(flow_state, 0)
    section_two = 0.75 * flow_state + 0.25 * (section_one + TIME_STEP * evaluate(section_one, 1))
    return 1.0 / 3.0 * flow_state + 2.0 / 3.0 * (section_two + TIME_STEP * evaluate(section_two, 2))


def solution(mesh):
    placed = (
        P(None, "row", None, "circ"),
        P(None, "row", None, "circ"),
        P(),
        P(),
        P("row", None, "circ"),
        P("row", None, "circ"),
    )
    return jax.shard_map(
        local, mesh=mesh, in_specs=placed, out_specs=P(None, "row", None, "circ"), check_vma=False
    )
```

```python
import jax
import jax.numpy as jnp
from jax import lax
from jax.sharding import PartitionSpec as P

SMAG_COEF = 0.1
TIME_STEP = 0.25
RADICES = (8, 4)


def tendency(center, below, above, around, velocity):
    radial = jnp.concatenate([center[:, :, :1], center, center[:, :, -1:]], axis=2)
    d_axial = 0.5 * (above - below)
    d_radial = 0.5 * (radial[:, :, 2:] - radial[:, :, :-2])
    d_around = 0.5 * (around[..., 2:] - around[..., :-2])
    laplace = (
        above
        + below
        + radial[:, :, 2:]
        + radial[:, :, :-2]
        + around[..., 2:]
        + around[..., :-2]
        - 6.0 * center
    )
    strain = jnp.sum(d_axial[1:4] ** 2 + d_radial[1:4] ** 2 + d_around[1:4] ** 2, axis=0)
    eddy_visc = SMAG_COEF * jnp.sqrt(strain + 1.0)
    return eddy_visc * laplace - (
        velocity[0] * d_axial + velocity[1] * d_radial + velocity[2] * d_around
    )


def local(flow_state, velocity, offsets, passage_shift, donor_step, donor_weight):
    row_count = lax.axis_size("row")
    loop_size = lax.axis_size("circ")
    row_id = lax.axis_index("row")
    pitch_cells = flow_state.shape[-1]
    planes = flow_state.shape[1]
    loop_cells = pitch_cells * loop_size
    comps, radial = flow_state.shape[0], flow_state.shape[2]
    lower_src = jnp.maximum(row_id - 1, 0)
    upper_src = jnp.minimum(row_id + 1, row_count - 1)
    lower_face = jnp.maximum(row_id - 1, 0)
    upper_face = jnp.minimum(row_id, row_count - 2)
    sources = jnp.stack([lower_src, upper_src])

    def along_row(value, step):
        return lax.ppermute(
            value, "row", [(r + step, r) for r in range(row_count) if 0 <= r + step < row_count]
        )

    def along_circ(value, shift):
        return lax.ppermute(
            value, "circ", [((b + shift) % loop_size, b) for b in range(loop_size)]
        )

    def circ_halo(cells):
        count = loop_size
        head = cells[..., :1]
        tail = cells[..., -1:]
        return jnp.concatenate(
            [
                lax.ppermute(tail, "circ", [(i, (i + 1) % count) for i in range(count)]),
                cells,
                lax.ppermute(head, "circ", [((i + 1) % count, i) for i in range(count)]),
            ],
            axis=-1,
        )

    def picks(section_index):
        low_offset = offsets[section_index, lower_face]
        high_offset = (loop_cells - offsets[section_index, upper_face]) % loop_cells
        offs = jnp.stack([low_offset, high_offset])
        coarse = offs // pitch_cells
        fine = offs % pitch_cells
        dq = (coarse + passage_shift[sources] - passage_shift[row_id]) % loop_size
        first_col = jnp.arange(pitch_cells, dtype=jnp.int32)[None, :] + fine[:, None] + donor_step[0]
        weights = donor_weight[0]
        rows = jnp.arange(3 * pitch_cells, dtype=jnp.int32)[None, :, None]
        pick = jnp.where(rows == first_col[:, None, :], weights[:, None, :], 0.0) + jnp.where(
            rows == first_col[:, None, :] + 1, 1.0 - weights[:, None, :], 0.0
        )
        return dq, pick.reshape(2, 3, pitch_cells, pitch_cells)

    def ghosts(last_plane, first_plane, section_index):
        dq, pick = picks(section_index)
        faces = jnp.stack([along_row(last_plane, -1), along_row(first_plane, 1)])
        first = RADICES[0]
        got = [faces] + [along_circ(faces, j) for j in range(1, first + 2)]
        digit = dq % first
        stack = jnp.stack(
            [
                jnp.stack([lax.select_n(digit[d], *[g[d] for g in got[i : i + first]]) for i in range(3)])
                for d in range(2)
            ]
        )
        span = first
        rest = dq // first
        for radix in RADICES[1:]:
            digit = rest % radix
            rest = rest // radix
            got = [stack] + [along_circ(stack, span * c) for c in range(1, radix)]
            stack = jnp.stack([lax.select_n(digit[d], *[g[d] for g in got]) for d in range(2)])
            span *= radix
        win = stack.reshape(2, 3, comps * radial, pitch_cells)
        out = jnp.einsum("dimk,dikn->dimn", win, pick, precision=lax.Precision.HIGHEST).sum(axis=1)
        out = out.reshape(2, comps, radial, pitch_cells)
        lower = jnp.where(row_id == 0, first_plane, out[0])
        upper = jnp.where(row_id == row_count - 1, last_plane, out[1])
        return lower, upper

    def section(fields, first_plane, last_plane, section_index, base_scale, step_scale):
        lower, upper = ghosts(last_plane, first_plane, section_index)
        around = circ_halo(fields)
        edge_idx = jnp.array([0, planes - 1])
        center = jnp.stack([first_plane, last_plane], axis=1)
        below = jnp.stack([lower, fields[:, planes - 2]], axis=1)
        above = jnp.stack([fields[:, 1], upper], axis=1)
        edge_rate = tendency(center, below, above, around[:, edge_idx], velocity[:, edge_idx])
        inner_rate = tendency(
            fields[:, 1:-1], fields[:, :-2], fields[:, 2:], around[:, 1:-1], velocity[:, 1:-1]
        )
        q_edge = flow_state[:, edge_idx]
        if base_scale is None:
            edge_next = center + TIME_STEP * edge_rate
            inner_next = fields[:, 1:-1] + TIME_STEP * inner_rate
        else:
            edge_next = base_scale * q_edge + step_scale * (center + TIME_STEP * edge_rate)
            inner_next = base_scale * flow_state[:, 1:-1] + step_scale * (
                fields[:, 1:-1] + TIME_STEP * inner_rate
            )
        nxt = jnp.concatenate([edge_next[:, :1], inner_next, edge_next[:, 1:]], axis=1)
        return nxt, edge_next[:, 0], edge_next[:, 1]

    v1, f1, l1 = section(flow_state, flow_state[:, 0], flow_state[:, -1], 0, None, None)
    v2, f2, l2 = section(v1, f1, l1, 1, 0.75, 0.25)
    v3, _, _ = section(v2, f2, l2, 2, 1.0 / 3.0, 2.0 / 3.0)
    return v3


def solution(mesh):
    placed = (
        P(None, "row", None, "circ"),
        P(None, "row", None, "circ"),
        P(),
        P(),
        P("row", None, "circ"),
        P("row", None, "circ"),
    )
    return jax.shard_map(
        local, mesh=mesh, in_specs=placed, out_specs=P(None, "row", None, "circ"), check_vma=False
    )
```

```python
import jax
import jax.numpy as jnp
from jax import lax
from jax.sharding import PartitionSpec as P

SMAG_COEF = 0.1
TIME_STEP = 0.25
RADICES = (8, 4)


def tendency(center, below, above, around, velocity):
    radial = jnp.concatenate([center[:, :, :1], center, center[:, :, -1:]], axis=2)
    d_axial = 0.5 * (above - below)
    d_radial = 0.5 * (radial[:, :, 2:] - radial[:, :, :-2])
    d_around = 0.5 * (around[..., 2:] - around[..., :-2])
    laplace = (
        above
        + below
        + radial[:, :, 2:]
        + radial[:, :, :-2]
        + around[..., 2:]
        + around[..., :-2]
        - 6.0 * center
    )
    strain = jnp.sum(d_axial[1:4] ** 2 + d_radial[1:4] ** 2 + d_around[1:4] ** 2, axis=0)
    eddy_visc = SMAG_COEF * jnp.sqrt(strain + 1.0)
    return eddy_visc * laplace - (
        velocity[0] * d_axial + velocity[1] * d_radial + velocity[2] * d_around
    )


def local(flow_state, velocity, offsets, passage_shift, donor_step, donor_weight):
    row_count = lax.axis_size("row")
    loop_size = lax.axis_size("circ")
    row_id = lax.axis_index("row")
    pitch_cells = flow_state.shape[-1]
    planes = flow_state.shape[1]
    loop_cells = pitch_cells * loop_size
    comps, radial = flow_state.shape[0], flow_state.shape[2]
    lower_src = jnp.maximum(row_id - 1, 0)
    upper_src = jnp.minimum(row_id + 1, row_count - 1)
    lower_face = jnp.maximum(row_id - 1, 0)
    upper_face = jnp.minimum(row_id, row_count - 2)
    sources = jnp.stack([lower_src, upper_src])

    def along_circ(value, shift):
        return lax.ppermute(
            value, "circ", [((b + shift) % loop_size, b) for b in range(loop_size)]
        )

    def circ_halo(cells):
        count = loop_size
        head = cells[..., :1]
        tail = cells[..., -1:]
        return jnp.concatenate(
            [
                lax.ppermute(tail, "circ", [(i, (i + 1) % count) for i in range(count)]),
                cells,
                lax.ppermute(head, "circ", [((i + 1) % count, i) for i in range(count)]),
            ],
            axis=-1,
        )

    def picks(section_index):
        low_offset = offsets[section_index, lower_face]
        high_offset = (loop_cells - offsets[section_index, upper_face]) % loop_cells
        offs = jnp.stack([low_offset, high_offset])
        coarse = offs // pitch_cells
        fine = offs % pitch_cells
        dq = (coarse + passage_shift[sources] - passage_shift[row_id]) % loop_size
        first_col = jnp.arange(pitch_cells, dtype=jnp.int32)[None, :] + fine[:, None] + donor_step[0]
        weights = donor_weight[0]
        rows = jnp.arange(3 * pitch_cells, dtype=jnp.int32)[None, :, None]
        pick = jnp.where(rows == first_col[:, None, :], weights[:, None, :], 0.0) + jnp.where(
            rows == first_col[:, None, :] + 1, 1.0 - weights[:, None, :], 0.0
        )
        return dq, pick.reshape(2, 3, pitch_cells, pitch_cells)

    def from_row(plane, step, shift):
        pairs = []
        for r in range(row_count):
            src = r + step
            if 0 <= src < row_count:
                for b in range(loop_size):
                    pairs.append((src * loop_size + (b + shift) % loop_size, r * loop_size + b))
        return lax.ppermute(plane, ("row", "circ"), pairs)

    def ghosts(last_plane, first_plane, section_index):
        dq, pick = picks(section_index)
        first = RADICES[0]
        digit = dq % first
        blocks = []
        for d, (plane, step) in enumerate(((last_plane, -1), (first_plane, 1))):
            got = [from_row(plane, step, j) for j in range(first + 2)]
            blocks.append(jnp.stack([lax.select_n(digit[d], *got[i : i + first]) for i in range(3)]))
        stack = jnp.stack(blocks)
        span = first
        rest = dq // first
        for radix in RADICES[1:]:
            digit = rest % radix
            rest = rest // radix
            got = [stack] + [along_circ(stack, span * c) for c in range(1, radix)]
            stack = jnp.stack([lax.select_n(digit[d], *[g[d] for g in got]) for d in range(2)])
            span *= radix
        win = stack.reshape(2, 3, comps * radial, pitch_cells)
        out = jnp.einsum("dimk,dikn->dimn", win, pick, precision=lax.Precision.HIGHEST).sum(axis=1)
        out = out.reshape(2, comps, radial, pitch_cells)
        lower = jnp.where(row_id == 0, first_plane, out[0])
        upper = jnp.where(row_id == row_count - 1, last_plane, out[1])
        return lower, upper

    def section(fields, first_plane, last_plane, section_index, base_scale, step_scale):
        lower, upper = ghosts(last_plane, first_plane, section_index)
        around = circ_halo(fields)
        edge_idx = jnp.array([0, planes - 1])
        center = jnp.stack([first_plane, last_plane], axis=1)
        below = jnp.stack([lower, fields[:, planes - 2]], axis=1)
        above = jnp.stack([fields[:, 1], upper], axis=1)
        edge_rate = tendency(center, below, above, around[:, edge_idx], velocity[:, edge_idx])
        inner_rate = tendency(
            fields[:, 1:-1], fields[:, :-2], fields[:, 2:], around[:, 1:-1], velocity[:, 1:-1]
        )
        q_edge = flow_state[:, edge_idx]
        if base_scale is None:
            edge_next = center + TIME_STEP * edge_rate
            inner_next = fields[:, 1:-1] + TIME_STEP * inner_rate
        else:
            edge_next = base_scale * q_edge + step_scale * (center + TIME_STEP * edge_rate)
            inner_next = base_scale * flow_state[:, 1:-1] + step_scale * (
                fields[:, 1:-1] + TIME_STEP * inner_rate
            )
        nxt = jnp.concatenate([edge_next[:, :1], inner_next, edge_next[:, 1:]], axis=1)
        return nxt, edge_next[:, 0], edge_next[:, 1]

    v1, f1, l1 = section(flow_state, flow_state[:, 0], flow_state[:, -1], 0, None, None)
    v2, f2, l2 = section(v1, f1, l1, 1, 0.75, 0.25)
    v3, _, _ = section(v2, f2, l2, 2, 1.0 / 3.0, 2.0 / 3.0)
    return v3


def solution(mesh):
    placed = (
        P(None, "row", None, "circ"),
        P(None, "row", None, "circ"),
        P(),
        P(),
        P("row", None, "circ"),
        P("row", None, "circ"),
    )
    return jax.shard_map(
        local, mesh=mesh, in_specs=placed, out_specs=P(None, "row", None, "circ"), check_vma=False
    )
```

```python
import jax
import jax.numpy as jnp
from jax import lax
from jax.sharding import PartitionSpec as P

SMAG_COEF = 0.1
TIME_STEP = 0.25
RADICES = (8, 4)


def extended(cells, sides, width):
    for axis, dim in sides:
        count = lax.axis_size(axis)
        head = lax.slice_in_dim(cells, 0, width, axis=dim)
        tail = lax.slice_in_dim(cells, cells.shape[dim] - width, cells.shape[dim], axis=dim)
        cells = jnp.concatenate(
            [
                lax.ppermute(tail, axis, [(i, (i + 1) % count) for i in range(count)]),
                cells,
                lax.ppermute(head, axis, [((i + 1) % count, i) for i in range(count)]),
            ],
            axis=dim,
        )
    return cells


def combine(fields, axial_ext, radial_ext, around_ext, velocity):
    d_axial = 0.5 * (axial_ext[:, 2:] - axial_ext[:, :-2])
    d_radial = 0.5 * (radial_ext[:, :, 2:] - radial_ext[:, :, :-2])
    d_around = 0.5 * (around_ext[..., 2:] - around_ext[..., :-2])
    laplace = (
        axial_ext[:, 2:]
        + axial_ext[:, :-2]
        + radial_ext[:, :, 2:]
        + radial_ext[:, :, :-2]
        + around_ext[..., 2:]
        + around_ext[..., :-2]
        - 6.0 * fields
    )
    strain = jnp.sum(d_axial[1:4] ** 2 + d_radial[1:4] ** 2 + d_around[1:4] ** 2, axis=0)
    eddy_visc = SMAG_COEF * jnp.sqrt(strain + 1.0)
    return eddy_visc * laplace - (
        velocity[0] * d_axial + velocity[1] * d_radial + velocity[2] * d_around
    )


def radial_pad(fields):
    return jnp.concatenate([fields[:, :, :1], fields, fields[:, :, -1:]], axis=2)


def axial_pad(fields, lower_ghost, upper_ghost):
    return jnp.concatenate([lower_ghost[:, None], fields, upper_ghost[:, None]], axis=1)


def local(flow_state, velocity, offsets, passage_shift, donor_step, donor_weight):
    row_count = lax.axis_size("row")
    loop_size = lax.axis_size("circ")
    row_id = lax.axis_index("row")
    pitch_cells = flow_state.shape[-1]
    loop_cells = pitch_cells * loop_size
    lower_src = jnp.maximum(row_id - 1, 0)
    upper_src = jnp.minimum(row_id + 1, row_count - 1)
    lower_face = jnp.maximum(row_id - 1, 0)
    upper_face = jnp.minimum(row_id, row_count - 2)
    window = 3 * pitch_cells

    def from_row(plane, step, shift):
        pairs = []
        for r in range(row_count):
            src = r + step
            if 0 <= src < row_count:
                for b in range(loop_size):
                    pairs.append((src * loop_size + (b + shift) % loop_size, r * loop_size + b))
        return lax.ppermute(plane, ("row", "circ"), pairs)

    def along_circ(value, shift):
        return lax.ppermute(
            value, "circ", [((b + shift) % loop_size, b) for b in range(loop_size)]
        )

    def picks(section_index):
        low_offset = offsets[section_index, lower_face]
        high_offset = (loop_cells - offsets[section_index, upper_face]) % loop_cells
        offs = jnp.stack([low_offset, high_offset])
        coarse = offs // pitch_cells
        fine = offs % pitch_cells
        sources = jnp.stack([lower_src, upper_src])
        dq = (coarse + passage_shift[sources] - passage_shift[row_id]) % loop_size
        first_col = (
            jnp.arange(pitch_cells, dtype=jnp.int32)[None, :] + fine[:, None] + donor_step[0]
        )
        weights = donor_weight[0]
        rows = jnp.arange(window, dtype=jnp.int32)[None, :, None]
        pick = jnp.where(rows == first_col[:, None, :], weights[:, None, :], 0.0) + jnp.where(
            rows == first_col[:, None, :] + 1, 1.0 - weights[:, None, :], 0.0
        )
        return dq, pick.reshape(2, 3, pitch_cells, pitch_cells)

    def ghosts(last_plane, first_plane, section_index):
        dq, pick = picks(section_index)
        first = RADICES[0]
        digit = dq % first
        blocks = []
        for d, (plane, step) in enumerate(((last_plane, -1), (first_plane, 1))):
            got = [from_row(plane, step, j) for j in range(first + 2)]
            blocks.append(jnp.stack([lax.select_n(digit[d], *got[i : i + first]) for i in range(3)]))
        stack = jnp.stack(blocks)
        span = first
        rest = dq // first
        for radix in RADICES[1:]:
            digit = rest % radix
            rest = rest // radix
            got = [stack] + [along_circ(stack, span * c) for c in range(1, radix)]
            stack = jnp.stack([lax.select_n(digit[d], *[g[d] for g in got]) for d in range(2)])
            span *= radix
        comps, radial = last_plane.shape[0], last_plane.shape[1]
        win = stack.reshape(2, 3, comps * radial, pitch_cells)
        out = jnp.einsum("dimk,dikn->dimn", win, pick, precision=lax.Precision.HIGHEST).sum(axis=1)
        out = out.reshape(2, comps, radial, pitch_cells)
        return out[0], out[1]

    def evaluate(fields, section_index):
        first_plane = fields[:, 0]
        last_plane = fields[:, -1]
        lower_ghost, upper_ghost = ghosts(last_plane, first_plane, section_index)
        lower_ghost = jnp.where(row_id == 0, first_plane, lower_ghost)
        upper_ghost = jnp.where(row_id == row_count - 1, last_plane, upper_ghost)
        around_ext = extended(fields, (("circ", 3),), 1)
        return combine(
            fields,
            axial_pad(fields, lower_ghost, upper_ghost),
            radial_pad(fields),
            around_ext,
            velocity,
        )

    section_one = flow_state + TIME_STEP * evaluate(flow_state, 0)
    section_two = 0.75 * flow_state + 0.25 * (section_one + TIME_STEP * evaluate(section_one, 1))
    return 1.0 / 3.0 * flow_state + 2.0 / 3.0 * (section_two + TIME_STEP * evaluate(section_two, 2))


def solution(mesh):
    placed = (
        P(None, "row", None, "circ"),
        P(None, "row", None, "circ"),
        P(),
        P(),
        P("row", None, "circ"),
        P("row", None, "circ"),
    )
    return jax.shard_map(
        local, mesh=mesh, in_specs=placed, out_specs=P(None, "row", None, "circ"), check_vma=False
    )
```

```python
import jax
import jax.numpy as jnp
from jax import lax
from jax.sharding import PartitionSpec as P

SMAG_COEF = 0.1
TIME_STEP = 0.25
RADICES = (8, 4)


def combine(fields, axial_ext, radial_ext, around_ext, velocity):
    d_axial = 0.5 * (axial_ext[:, 2:] - axial_ext[:, :-2])
    d_radial = 0.5 * (radial_ext[:, :, 2:] - radial_ext[:, :, :-2])
    d_around = 0.5 * (around_ext[..., 2:] - around_ext[..., :-2])
    laplace = (
        axial_ext[:, 2:]
        + axial_ext[:, :-2]
        + radial_ext[:, :, 2:]
        + radial_ext[:, :, :-2]
        + around_ext[..., 2:]
        + around_ext[..., :-2]
        - 6.0 * fields
    )
    strain = jnp.sum(d_axial[1:4] ** 2 + d_radial[1:4] ** 2 + d_around[1:4] ** 2, axis=0)
    eddy_visc = SMAG_COEF * jnp.sqrt(strain + 1.0)
    return eddy_visc * laplace - (
        velocity[0] * d_axial + velocity[1] * d_radial + velocity[2] * d_around
    )


def radial_pad(fields):
    return jnp.concatenate([fields[:, :, :1], fields, fields[:, :, -1:]], axis=2)


def axial_pad(fields, lower_ghost, upper_ghost):
    return jnp.concatenate([lower_ghost[:, None], fields, upper_ghost[:, None]], axis=1)


def local(flow_state, velocity, offsets, passage_shift, donor_step, donor_weight):
    row_count = lax.axis_size("row")
    loop_size = lax.axis_size("circ")
    row_id = lax.axis_index("row")
    pitch_cells = flow_state.shape[-1]
    planes = flow_state.shape[1]
    loop_cells = pitch_cells * loop_size
    comps, radial = flow_state.shape[0], flow_state.shape[2]
    lower_src = jnp.maximum(row_id - 1, 0)
    upper_src = jnp.minimum(row_id + 1, row_count - 1)
    lower_face = jnp.maximum(row_id - 1, 0)
    upper_face = jnp.minimum(row_id, row_count - 2)
    sources = jnp.stack([lower_src, upper_src])

    def along_row(value, step):
        return lax.ppermute(
            value, "row", [(r + step, r) for r in range(row_count) if 0 <= r + step < row_count]
        )

    def along_circ(value, shift):
        return lax.ppermute(
            value, "circ", [((b + shift) % loop_size, b) for b in range(loop_size)]
        )

    def circ_halo(cells):
        count = loop_size
        head = cells[..., :1]
        tail = cells[..., -1:]
        return jnp.concatenate(
            [
                lax.ppermute(tail, "circ", [(i, (i + 1) % count) for i in range(count)]),
                cells,
                lax.ppermute(head, "circ", [((i + 1) % count, i) for i in range(count)]),
            ],
            axis=-1,
        )

    def picks(section_index):
        low_offset = offsets[section_index, lower_face]
        high_offset = (loop_cells - offsets[section_index, upper_face]) % loop_cells
        offs = jnp.stack([low_offset, high_offset])
        coarse = offs // pitch_cells
        fine = offs % pitch_cells
        dq = (coarse + passage_shift[sources] - passage_shift[row_id]) % loop_size
        first_col = jnp.arange(pitch_cells, dtype=jnp.int32)[None, :] + fine[:, None] + donor_step[0]
        weights = donor_weight[0]
        rows = jnp.arange(3 * pitch_cells, dtype=jnp.int32)[None, :, None]
        pick = jnp.where(rows == first_col[:, None, :], weights[:, None, :], 0.0) + jnp.where(
            rows == first_col[:, None, :] + 1, 1.0 - weights[:, None, :], 0.0
        )
        return dq, pick.reshape(2, 3, pitch_cells, pitch_cells)

    def ghosts(last_plane, first_plane, section_index, fields):
        dq, pick = picks(section_index)
        faces = jnp.stack([along_row(last_plane, -1), along_row(first_plane, 1)])
        around = circ_halo(fields)
        faces, around = lax.optimization_barrier((faces, around))
        first = RADICES[0]
        got = [faces] + [along_circ(faces, j) for j in range(1, first + 2)]
        digit = dq % first
        stack = jnp.stack(
            [
                jnp.stack([lax.select_n(digit[d], *[g[d] for g in got[i : i + first]]) for i in range(3)])
                for d in range(2)
            ]
        )
        span = first
        rest = dq // first
        for radix in RADICES[1:]:
            digit = rest % radix
            rest = rest // radix
            got = [stack] + [along_circ(stack, span * c) for c in range(1, radix)]
            stack = jnp.stack([lax.select_n(digit[d], *[g[d] for g in got]) for d in range(2)])
            span *= radix
        win = stack.reshape(2, 3, comps * radial, pitch_cells)
        out = [
            sum(
                jnp.dot(win[d, i], pick[d, i], precision=lax.Precision.HIGHEST) for i in range(3)
            ).reshape(comps, radial, pitch_cells)
            for d in range(2)
        ]
        lower = jnp.where(row_id == 0, first_plane, out[0])
        upper = jnp.where(row_id == row_count - 1, last_plane, out[1])
        return lower, upper, around

    def evaluate(fields, section_index):
        first_plane = fields[:, 0]
        last_plane = fields[:, -1]
        lower_ghost, upper_ghost, around_ext = ghosts(last_plane, first_plane, section_index, fields)
        return combine(
            fields,
            axial_pad(fields, lower_ghost, upper_ghost),
            radial_pad(fields),
            around_ext,
            velocity,
        )

    section_one = flow_state + TIME_STEP * evaluate(flow_state, 0)
    section_two = 0.75 * flow_state + 0.25 * (section_one + TIME_STEP * evaluate(section_one, 1))
    return 1.0 / 3.0 * flow_state + 2.0 / 3.0 * (section_two + TIME_STEP * evaluate(section_two, 2))


def solution(mesh):
    placed = (
        P(None, "row", None, "circ"),
        P(None, "row", None, "circ"),
        P(),
        P(),
        P("row", None, "circ"),
        P("row", None, "circ"),
    )
    return jax.shard_map(
        local, mesh=mesh, in_specs=placed, out_specs=P(None, "row", None, "circ"), check_vma=False
    )
```

```python
import jax
import jax.numpy as jnp
from jax import lax
from jax.sharding import PartitionSpec as P

SMAG_COEF = 0.1
TIME_STEP = 0.25
RADICES = (8,)


def combine(fields, axial_ext, radial_ext, around_ext, velocity):
    d_axial = 0.5 * (axial_ext[:, 2:] - axial_ext[:, :-2])
    d_radial = 0.5 * (radial_ext[:, :, 2:] - radial_ext[:, :, :-2])
    d_around = 0.5 * (around_ext[..., 2:] - around_ext[..., :-2])
    laplace = (
        axial_ext[:, 2:]
        + axial_ext[:, :-2]
        + radial_ext[:, :, 2:]
        + radial_ext[:, :, :-2]
        + around_ext[..., 2:]
        + around_ext[..., :-2]
        - 6.0 * fields
    )
    strain = jnp.sum(d_axial[1:4] ** 2 + d_radial[1:4] ** 2 + d_around[1:4] ** 2, axis=0)
    eddy_visc = SMAG_COEF * jnp.sqrt(strain + 1.0)
    return eddy_visc * laplace - (
        velocity[0] * d_axial + velocity[1] * d_radial + velocity[2] * d_around
    )


def radial_pad(fields):
    return jnp.concatenate([fields[:, :, :1], fields, fields[:, :, -1:]], axis=2)


def axial_pad(fields, lower_ghost, upper_ghost):
    return jnp.concatenate([lower_ghost[:, None], fields, upper_ghost[:, None]], axis=1)


def local(flow_state, velocity, offsets, passage_shift, donor_step, donor_weight):
    row_count = lax.axis_size("row")
    loop_size = lax.axis_size("circ")
    row_id = lax.axis_index("row")
    pitch_cells = flow_state.shape[-1]
    planes = flow_state.shape[1]
    loop_cells = pitch_cells * loop_size
    comps, radial = flow_state.shape[0], flow_state.shape[2]
    lower_src = jnp.maximum(row_id - 1, 0)
    upper_src = jnp.minimum(row_id + 1, row_count - 1)
    lower_face = jnp.maximum(row_id - 1, 0)
    upper_face = jnp.minimum(row_id, row_count - 2)
    sources = jnp.stack([lower_src, upper_src])

    def from_row(plane, step, shift):
        pairs = []
        for r in range(row_count):
            src = r + step
            if 0 <= src < row_count:
                for b in range(loop_size):
                    pairs.append((src * loop_size + (b + shift) % loop_size, r * loop_size + b))
        return lax.ppermute(plane, ("row", "circ"), pairs)

    def along_circ(value, shift):
        return lax.ppermute(
            value, "circ", [((b + shift) % loop_size, b) for b in range(loop_size)]
        )

    def circ_halo(cells):
        count = loop_size
        head = cells[..., :1]
        tail = cells[..., -1:]
        return jnp.concatenate(
            [
                lax.ppermute(tail, "circ", [(i, (i + 1) % count) for i in range(count)]),
                cells,
                lax.ppermute(head, "circ", [((i + 1) % count, i) for i in range(count)]),
            ],
            axis=-1,
        )

    def picks(section_index):
        low_offset = offsets[section_index, lower_face]
        high_offset = (loop_cells - offsets[section_index, upper_face]) % loop_cells
        offs = jnp.stack([low_offset, high_offset])
        coarse = offs // pitch_cells
        fine = offs % pitch_cells
        dq = (coarse + passage_shift[sources] - passage_shift[row_id]) % loop_size
        first_col = jnp.arange(pitch_cells, dtype=jnp.int32)[None, :] + fine[:, None] + donor_step[0]
        weights = donor_weight[0]
        rows = jnp.arange(3 * pitch_cells, dtype=jnp.int32)[None, :, None]
        pick = jnp.where(rows == first_col[:, None, :], weights[:, None, :], 0.0) + jnp.where(
            rows == first_col[:, None, :] + 1, 1.0 - weights[:, None, :], 0.0
        )
        return dq, pick.reshape(2, 3, pitch_cells, pitch_cells)

    def ghosts(last_plane, first_plane, section_index, fields):
        dq, pick = picks(section_index)
        fine = RADICES[0]
        coarse = dq // fine
        digit = dq % fine
        moved = []
        for d, (plane, step) in enumerate(((last_plane, -1), (first_plane, 1))):
            got = [from_row(plane, step, fine * c) for c in range(loop_size // fine)]
            moved.append(lax.select_n(coarse[d], *got))
        faces = jnp.stack(moved)
        around = circ_halo(fields)
        faces, around = lax.optimization_barrier((faces, around))
        got = [faces] + [along_circ(faces, j) for j in range(1, fine + 2)]
        stack = jnp.stack(
            [
                jnp.stack([lax.select_n(digit[d], *[g[d] for g in got[i : i + fine]]) for i in range(3)])
                for d in range(2)
            ]
        )
        win = stack.reshape(2, 3, comps * radial, pitch_cells)
        out = [
            sum(
                jnp.dot(win[d, i], pick[d, i], precision=lax.Precision.HIGHEST) for i in range(3)
            ).reshape(comps, radial, pitch_cells)
            for d in range(2)
        ]
        lower = jnp.where(row_id == 0, first_plane, out[0])
        upper = jnp.where(row_id == row_count - 1, last_plane, out[1])
        return lower, upper, around

    def evaluate(fields, section_index):
        first_plane = fields[:, 0]
        last_plane = fields[:, -1]
        lower_ghost, upper_ghost, around_ext = ghosts(last_plane, first_plane, section_index, fields)
        return combine(
            fields,
            axial_pad(fields, lower_ghost, upper_ghost),
            radial_pad(fields),
            around_ext,
            velocity,
        )

    section_one = flow_state + TIME_STEP * evaluate(flow_state, 0)
    section_two = 0.75 * flow_state + 0.25 * (section_one + TIME_STEP * evaluate(section_one, 1))
    return 1.0 / 3.0 * flow_state + 2.0 / 3.0 * (section_two + TIME_STEP * evaluate(section_two, 2))


def solution(mesh):
    placed = (
        P(None, "row", None, "circ"),
        P(None, "row", None, "circ"),
        P(),
        P(),
        P("row", None, "circ"),
        P("row", None, "circ"),
    )
    return jax.shard_map(
        local, mesh=mesh, in_specs=placed, out_specs=P(None, "row", None, "circ"), check_vma=False
    )
```

```python
import jax
import jax.numpy as jnp
from jax import lax
from jax.sharding import PartitionSpec as P

SMAG_COEF = 0.1
TIME_STEP = 0.25
RADICES = (8, 4)


def extended(cells, sides, width):
    for axis, dim in sides:
        count = lax.axis_size(axis)
        head = lax.slice_in_dim(cells, 0, width, axis=dim)
        tail = lax.slice_in_dim(cells, cells.shape[dim] - width, cells.shape[dim], axis=dim)
        cells = jnp.concatenate(
            [
                lax.ppermute(tail, axis, [(i, (i + 1) % count) for i in range(count)]),
                cells,
                lax.ppermute(head, axis, [((i + 1) % count, i) for i in range(count)]),
            ],
            axis=dim,
        )
    return cells


def combine(fields, axial_ext, radial_ext, around_ext, velocity):
    d_axial = 0.5 * (axial_ext[:, 2:] - axial_ext[:, :-2])
    d_radial = 0.5 * (radial_ext[:, :, 2:] - radial_ext[:, :, :-2])
    d_around = 0.5 * (around_ext[..., 2:] - around_ext[..., :-2])
    laplace = (
        axial_ext[:, 2:]
        + axial_ext[:, :-2]
        + radial_ext[:, :, 2:]
        + radial_ext[:, :, :-2]
        + around_ext[..., 2:]
        + around_ext[..., :-2]
        - 6.0 * fields
    )
    strain = jnp.sum(d_axial[1:4] ** 2 + d_radial[1:4] ** 2 + d_around[1:4] ** 2, axis=0)
    eddy_visc = SMAG_COEF * jnp.sqrt(strain + 1.0)
    return eddy_visc * laplace - (
        velocity[0] * d_axial + velocity[1] * d_radial + velocity[2] * d_around
    )


def radial_pad(fields):
    return jnp.concatenate([fields[:, :, :1], fields, fields[:, :, -1:]], axis=2)


def axial_pad(fields, lower_ghost, upper_ghost):
    return jnp.concatenate([lower_ghost[:, None], fields, upper_ghost[:, None]], axis=1)


def local(flow_state, velocity, offsets, passage_shift, donor_step, donor_weight):
    row_count = lax.axis_size("row")
    loop_size = lax.axis_size("circ")
    row_id = lax.axis_index("row")
    pitch_cells = flow_state.shape[-1]
    loop_cells = pitch_cells * loop_size
    lower_src = jnp.maximum(row_id - 1, 0)
    upper_src = jnp.minimum(row_id + 1, row_count - 1)
    lower_face = jnp.maximum(row_id - 1, 0)
    upper_face = jnp.minimum(row_id, row_count - 2)
    window = 3 * pitch_cells

    def from_row(plane, step, shift):
        pairs = []
        for r in range(row_count):
            src = r + step
            if 0 <= src < row_count:
                for b in range(loop_size):
                    pairs.append((src * loop_size + (b + shift) % loop_size, r * loop_size + b))
        return lax.ppermute(plane, ("row", "circ"), pairs)

    def along_circ(value, shift):
        return lax.ppermute(
            value, "circ", [((b + shift) % loop_size, b) for b in range(loop_size)]
        )

    def picks(section_index):
        low_offset = offsets[section_index, lower_face]
        high_offset = (loop_cells - offsets[section_index, upper_face]) % loop_cells
        offs = jnp.stack([low_offset, high_offset])
        coarse = offs // pitch_cells
        fine = offs % pitch_cells
        sources = jnp.stack([lower_src, upper_src])
        dq = (coarse + passage_shift[sources] - passage_shift[row_id]) % loop_size
        first_col = (
            jnp.arange(pitch_cells, dtype=jnp.int32)[None, :] + fine[:, None] + donor_step[0]
        )
        weights = donor_weight[0]
        rows = jnp.arange(window, dtype=jnp.int32)[None, :, None]
        pick = jnp.where(rows == first_col[:, None, :], weights[:, None, :], 0.0) + jnp.where(
            rows == first_col[:, None, :] + 1, 1.0 - weights[:, None, :], 0.0
        )
        return dq, pick.reshape(2, 3, pitch_cells, pitch_cells)

    def ghosts(last_plane, first_plane, section_index):
        dq, pick = picks(section_index)
        first = RADICES[0]
        digit = dq % first
        blocks = []
        for d, (plane, step) in enumerate(((last_plane, -1), (first_plane, 1))):
            got = [from_row(plane, step, j) for j in range(first + 2)]
            blocks.append(jnp.stack([lax.select_n(digit[d], *got[i : i + first]) for i in range(3)]))
        stack = jnp.stack(blocks)
        span = first
        rest = dq // first
        for radix in RADICES[1:]:
            digit = rest % radix
            rest = rest // radix
            got = [stack] + [along_circ(stack, span * c) for c in range(1, radix)]
            stack = jnp.stack([lax.select_n(digit[d], *[g[d] for g in got]) for d in range(2)])
            span *= radix
        comps, radial = last_plane.shape[0], last_plane.shape[1]
        win = stack.reshape(2, 3, comps * radial, pitch_cells)
        out = [
            sum(
                jnp.dot(win[d, i], pick[d, i], precision=lax.Precision.HIGHEST) for i in range(3)
            ).reshape(comps, radial, pitch_cells)
            for d in range(2)
        ]
        return out[0], out[1]

    def evaluate(fields, section_index):
        first_plane = fields[:, 0]
        last_plane = fields[:, -1]
        lower_ghost, upper_ghost = ghosts(last_plane, first_plane, section_index)
        lower_ghost = jnp.where(row_id == 0, first_plane, lower_ghost)
        upper_ghost = jnp.where(row_id == row_count - 1, last_plane, upper_ghost)
        around_ext = extended(fields, (("circ", 3),), 1)
        return combine(
            fields,
            axial_pad(fields, lower_ghost, upper_ghost),
            radial_pad(fields),
            around_ext,
            velocity,
        )

    section_one = flow_state + TIME_STEP * evaluate(flow_state, 0)
    section_two = 0.75 * flow_state + 0.25 * (section_one + TIME_STEP * evaluate(section_one, 1))
    return 1.0 / 3.0 * flow_state + 2.0 / 3.0 * (section_two + TIME_STEP * evaluate(section_two, 2))


def solution(mesh):
    placed = (
        P(None, "row", None, "circ"),
        P(None, "row", None, "circ"),
        P(),
        P(),
        P("row", None, "circ"),
        P("row", None, "circ"),
    )
    return jax.shard_map(
        local, mesh=mesh, in_specs=placed, out_specs=P(None, "row", None, "circ"), check_vma=False
    )
```

```python
import jax
import jax.numpy as jnp
from jax import lax
from jax.sharding import PartitionSpec as P


SMAG_COEF = 0.1
TIME_STEP = 0.25
RADICES = (8, 4)


def extended(cells, sides, width):
    for axis, dim in sides:
        count = lax.axis_size(axis)
        head = lax.slice_in_dim(cells, 0, width, axis=dim)
        tail = lax.slice_in_dim(cells, cells.shape[dim] - width, cells.shape[dim], axis=dim)
        cells = jnp.concatenate(
            [
                lax.ppermute(tail, axis, [(i, (i + 1) % count) for i in range(count)]),
                cells,
                lax.ppermute(head, axis, [((i + 1) % count, i) for i in range(count)]),
            ],
            axis=dim,
        )
    return cells


def combine(fields, axial_ext, radial_ext, around_ext, velocity):
    d_axial = 0.5 * (axial_ext[:, 2:] - axial_ext[:, :-2])
    d_radial = 0.5 * (radial_ext[:, :, 2:] - radial_ext[:, :, :-2])
    d_around = 0.5 * (around_ext[..., 2:] - around_ext[..., :-2])
    laplace = (
        axial_ext[:, 2:]
        + axial_ext[:, :-2]
        + radial_ext[:, :, 2:]
        + radial_ext[:, :, :-2]
        + around_ext[..., 2:]
        + around_ext[..., :-2]
        - 6.0 * fields
    )
    strain = jnp.sum(d_axial[1:4] ** 2 + d_radial[1:4] ** 2 + d_around[1:4] ** 2, axis=0)
    eddy_visc = SMAG_COEF * jnp.sqrt(strain + 1.0)
    return eddy_visc * laplace - (
        velocity[0] * d_axial + velocity[1] * d_radial + velocity[2] * d_around
    )


def radial_pad(fields):
    return jnp.concatenate([fields[:, :, :1], fields, fields[:, :, -1:]], axis=2)


def axial_pad(fields, lower_ghost, upper_ghost):
    return jnp.concatenate([lower_ghost[:, None], fields, upper_ghost[:, None]], axis=1)


def local(flow_state, velocity, offsets, passage_shift, donor_step, donor_weight):
    row_count = lax.axis_size("row")
    loop_size = lax.axis_size("circ")
    row_id = lax.axis_index("row")
    pitch_cells = flow_state.shape[-1]
    loop_cells = pitch_cells * loop_size
    lower_src = jnp.maximum(row_id - 1, 0)
    upper_src = jnp.minimum(row_id + 1, row_count - 1)
    lower_face = jnp.maximum(row_id - 1, 0)
    upper_face = jnp.minimum(row_id, row_count - 2)
    window = 3 * pitch_cells

    def from_row(plane, step, shift):
        pairs = []
        for r in range(row_count):
            src = r + step
            if 0 <= src < row_count:
                for b in range(loop_size):
                    pairs.append((src * loop_size + (b + shift) % loop_size, r * loop_size + b))
        return lax.ppermute(plane, ("row", "circ"), pairs)

    def along_circ(value, shift):
        return lax.ppermute(
            value, "circ", [((b + shift) % loop_size, b) for b in range(loop_size)]
        )

    def picks(section_index):
        low_offset = offsets[section_index, lower_face]
        high_offset = (loop_cells - offsets[section_index, upper_face]) % loop_cells
        offs = jnp.stack([low_offset, high_offset])
        coarse = offs // pitch_cells
        fine = offs % pitch_cells
        sources = jnp.stack([lower_src, upper_src])
        dq = (coarse + passage_shift[sources] - passage_shift[row_id]) % loop_size
        first_col = (
            jnp.arange(pitch_cells, dtype=jnp.int32)[None, :] + fine[:, None] + donor_step[0]
        )
        weights = donor_weight[0]
        rows = jnp.arange(window, dtype=jnp.int32)[None, :, None]
        pick = jnp.where(rows == first_col[:, None, :], weights[:, None, :], 0.0) + jnp.where(
            rows == first_col[:, None, :] + 1, 1.0 - weights[:, None, :], 0.0
        )
        return dq, pick.reshape(2, 3, pitch_cells, pitch_cells)

    def ghosts(last_plane, first_plane, section_index):
        dq, pick = picks(section_index)
        first = RADICES[0]
        digit = dq % first
        blocks = []
        for d, (plane, step) in enumerate(((last_plane, -1), (first_plane, 1))):
            got = [from_row(plane, step, j) for j in range(first + 2)]
            blocks.append(jnp.stack([lax.select_n(digit[d], *got[i : i + first]) for i in range(3)]))
        stack = jnp.stack(blocks)
        span = first
        rest = dq // first
        for radix in RADICES[1:]:
            digit = rest % radix
            rest = rest // radix
            got = [stack] + [along_circ(stack, span * c) for c in range(1, radix)]
            stack = jnp.stack([lax.select_n(digit[d], *[g[d] for g in got]) for d in range(2)])
            span *= radix
        comps, radial = last_plane.shape[0], last_plane.shape[1]
        win = stack.reshape(2, 3, comps * radial, pitch_cells)
        out = [
            sum(
                jnp.dot(win[d, i], pick[d, i], precision=lax.Precision.HIGHEST) for i in range(3)
            ).reshape(comps, radial, pitch_cells)
            for d in range(2)
        ]
        return out[0], out[1]

    def evaluate_section(fields, section_index):
        first_plane = fields[:, 0]
        last_plane = fields[:, -1]
        around_ext = extended(fields, (("circ", 3),), 1)
        lower_ghost, upper_ghost = ghosts(last_plane, first_plane, section_index)
        lower_ghost = jnp.where(row_id == 0, first_plane, lower_ghost)
        upper_ghost = jnp.where(row_id == row_count - 1, last_plane, upper_ghost)
        return combine(
            fields,
            axial_pad(fields, lower_ghost, upper_ghost),
            radial_pad(fields),
            around_ext,
            velocity,
        )

    section_one = flow_state + TIME_STEP * evaluate_section(flow_state, 0)
    section_two = 0.75 * flow_state + 0.25 * (section_one + TIME_STEP * evaluate_section(section_one, 1))
    return 1.0 / 3.0 * flow_state + 2.0 / 3.0 * (section_two + TIME_STEP * evaluate_section(section_two, 2))


def solution(mesh):
    placed = (
        P(None, "row", None, "circ"),
        P(None, "row", None, "circ"),
        P(),
        P(),
        P("row", None, "circ"),
        P("row", None, "circ"),
    )
    return jax.shard_map(
        local, mesh=mesh, in_specs=placed, out_specs=P(None, "row", None, "circ"), check_vma=False
    )
```

```python
import jax
import jax.numpy as jnp
from jax import lax
from jax.sharding import PartitionSpec as P


SMAG_COEF = 0.1
TIME_STEP = 0.25
RADICES = (8, 4)


def extended(cells, sides, width):
    for axis, dim in sides:
        count = lax.axis_size(axis)
        head = lax.slice_in_dim(cells, 0, width, axis=dim)
        tail = lax.slice_in_dim(cells, cells.shape[dim] - width, cells.shape[dim], axis=dim)
        cells = jnp.concatenate(
            [
                lax.ppermute(tail, axis, [(i, (i + 1) % count) for i in range(count)]),
                cells,
                lax.ppermute(head, axis, [((i + 1) % count, i) for i in range(count)]),
            ],
            axis=dim,
        )
    return cells


def tendency(center, below, above, around, velocity):
    radial = jnp.concatenate([center[:, :, :1], center, center[:, :, -1:]], axis=2)
    d_axial = 0.5 * (above - below)
    d_radial = 0.5 * (radial[:, :, 2:] - radial[:, :, :-2])
    d_around = 0.5 * (around[..., 2:] - around[..., :-2])
    laplace = (
        above
        + below
        + radial[:, :, 2:]
        + radial[:, :, :-2]
        + around[..., 2:]
        + around[..., :-2]
        - 6.0 * center
    )
    strain = jnp.sum(d_axial[1:4] ** 2 + d_radial[1:4] ** 2 + d_around[1:4] ** 2, axis=0)
    eddy_visc = SMAG_COEF * jnp.sqrt(strain + 1.0)
    return eddy_visc * laplace - (
        velocity[0] * d_axial + velocity[1] * d_radial + velocity[2] * d_around
    )


def local(flow_state, velocity, offsets, passage_shift, donor_step, donor_weight):
    row_count = lax.axis_size("row")
    loop_size = lax.axis_size("circ")
    row_id = lax.axis_index("row")
    pitch_cells = flow_state.shape[-1]
    loop_cells = pitch_cells * loop_size
    lower_src = jnp.maximum(row_id - 1, 0)
    upper_src = jnp.minimum(row_id + 1, row_count - 1)
    lower_face = jnp.maximum(row_id - 1, 0)
    upper_face = jnp.minimum(row_id, row_count - 2)
    window = 3 * pitch_cells

    def from_row(plane, step, shift):
        pairs = []
        for r in range(row_count):
            src = r + step
            if 0 <= src < row_count:
                for b in range(loop_size):
                    pairs.append((src * loop_size + (b + shift) % loop_size, r * loop_size + b))
        return lax.ppermute(plane, ("row", "circ"), pairs)

    def along_circ(value, shift):
        return lax.ppermute(
            value, "circ", [((b + shift) % loop_size, b) for b in range(loop_size)]
        )

    def picks(section_index):
        low_offset = offsets[section_index, lower_face]
        high_offset = (loop_cells - offsets[section_index, upper_face]) % loop_cells
        offs = jnp.stack([low_offset, high_offset])
        coarse = offs // pitch_cells
        fine = offs % pitch_cells
        sources = jnp.stack([lower_src, upper_src])
        dq = (coarse + passage_shift[sources] - passage_shift[row_id]) % loop_size
        first_col = (
            jnp.arange(pitch_cells, dtype=jnp.int32)[None, :] + fine[:, None] + donor_step[0]
        )
        weights = donor_weight[0]
        rows = jnp.arange(window, dtype=jnp.int32)[None, :, None]
        pick = jnp.where(rows == first_col[:, None, :], weights[:, None, :], 0.0) + jnp.where(
            rows == first_col[:, None, :] + 1, 1.0 - weights[:, None, :], 0.0
        )
        return dq, pick.reshape(2, 3, pitch_cells, pitch_cells)

    def ghosts(last_plane, first_plane, section_index):
        dq, pick = picks(section_index)
        first = RADICES[0]
        digit = dq % first
        blocks = []
        for d, (plane, step) in enumerate(((last_plane, -1), (first_plane, 1))):
            got = [from_row(plane, step, j) for j in range(first + 2)]
            blocks.append(jnp.stack([lax.select_n(digit[d], *got[i : i + first]) for i in range(3)]))
        stack = jnp.stack(blocks)
        span = first
        rest = dq // first
        for radix in RADICES[1:]:
            digit = rest % radix
            rest = rest // radix
            got = [stack] + [along_circ(stack, span * c) for c in range(1, radix)]
            stack = jnp.stack([lax.select_n(digit[d], *[g[d] for g in got]) for d in range(2)])
            span *= radix
        comps, radial = last_plane.shape[0], last_plane.shape[1]
        win = stack.reshape(2, 3, comps * radial, pitch_cells)
        out = [
            sum(
                jnp.dot(win[d, i], pick[d, i], precision=lax.Precision.HIGHEST) for i in range(3)
            ).reshape(comps, radial, pitch_cells)
            for d in range(2)
        ]
        return out[0], out[1]

    def section(fields, first_plane, last_plane, section_index, base_scale, step_scale):
        around = extended(fields, (("circ", 3),), 1)
        lower, upper = ghosts(last_plane, first_plane, section_index)
        lower = jnp.where(row_id == 0, first_plane, lower)
        upper = jnp.where(row_id == row_count - 1, last_plane, upper)

        def advance(start, now, rate):
            if base_scale is None:
                return now + TIME_STEP * rate
            return base_scale * start + step_scale * (now + TIME_STEP * rate)

        head = advance(
            flow_state[:, :1],
            fields[:, :1],
            tendency(fields[:, :1], lower[:, None], fields[:, 1:2], around[:, :1], velocity[:, :1]),
        )
        tail = advance(
            flow_state[:, -1:],
            fields[:, -1:],
            tendency(
                fields[:, -1:], fields[:, -2:-1], upper[:, None], around[:, -1:], velocity[:, -1:]
            ),
        )
        inner = advance(
            flow_state[:, 1:-1],
            fields[:, 1:-1],
            tendency(
                fields[:, 1:-1], fields[:, :-2], fields[:, 2:], around[:, 1:-1], velocity[:, 1:-1]
            ),
        )
        return jnp.concatenate([head, inner, tail], axis=1), head[:, 0], tail[:, 0]

    v1, f1, l1 = section(flow_state, flow_state[:, 0], flow_state[:, -1], 0, None, None)
    v2, f2, l2 = section(v1, f1, l1, 1, 0.75, 0.25)
    v3, _, _ = section(v2, f2, l2, 2, 1.0 / 3.0, 2.0 / 3.0)
    return v3


def solution(mesh):
    placed = (
        P(None, "row", None, "circ"),
        P(None, "row", None, "circ"),
        P(),
        P(),
        P("row", None, "circ"),
        P("row", None, "circ"),
    )
    return jax.shard_map(
        local, mesh=mesh, in_specs=placed, out_specs=P(None, "row", None, "circ"), check_vma=False
    )
```

```python
import jax
import jax.numpy as jnp
from jax import lax
from jax.sharding import PartitionSpec as P

SMAG_COEF = 0.1
TIME_STEP = 0.25
RADICES = (8, 4)


def extended(cells, sides, width):
    for axis, dim in sides:
        count = lax.axis_size(axis)
        head = lax.slice_in_dim(cells, 0, width, axis=dim)
        tail = lax.slice_in_dim(cells, cells.shape[dim] - width, cells.shape[dim], axis=dim)
        cells = jnp.concatenate(
            [
                lax.ppermute(tail, axis, [(i, (i + 1) % count) for i in range(count)]),
                cells,
                lax.ppermute(head, axis, [((i + 1) % count, i) for i in range(count)]),
            ],
            axis=dim,
        )
    return cells


def combine(fields, axial_ext, radial_ext, around_ext, velocity):
    d_axial = 0.5 * (axial_ext[:, 2:] - axial_ext[:, :-2])
    d_radial = 0.5 * (radial_ext[:, :, 2:] - radial_ext[:, :, :-2])
    d_around = 0.5 * (around_ext[..., 2:] - around_ext[..., :-2])
    laplace = (
        axial_ext[:, 2:]
        + axial_ext[:, :-2]
        + radial_ext[:, :, 2:]
        + radial_ext[:, :, :-2]
        + around_ext[..., 2:]
        + around_ext[..., :-2]
        - 6.0 * fields
    )
    strain = jnp.sum(d_axial[1:4] ** 2 + d_radial[1:4] ** 2 + d_around[1:4] ** 2, axis=0)
    eddy_visc = SMAG_COEF * jnp.sqrt(strain + 1.0)
    return eddy_visc * laplace - (
        velocity[0] * d_axial + velocity[1] * d_radial + velocity[2] * d_around
    )


def radial_pad(fields):
    return jnp.concatenate([fields[:, :, :1], fields, fields[:, :, -1:]], axis=2)


def axial_pad(fields, lower_ghost, upper_ghost):
    return jnp.concatenate([lower_ghost[:, None], fields, upper_ghost[:, None]], axis=1)


def local(flow_state, velocity, offsets, passage_shift, donor_step, donor_weight):
    row_count = lax.axis_size("row")
    loop_size = lax.axis_size("circ")
    row_id = lax.axis_index("row")
    pitch_cells = flow_state.shape[-1]
    loop_cells = pitch_cells * loop_size
    lower_src = jnp.maximum(row_id - 1, 0)
    upper_src = jnp.minimum(row_id + 1, row_count - 1)
    lower_face = jnp.maximum(row_id - 1, 0)
    upper_face = jnp.minimum(row_id, row_count - 2)
    window = 2 * pitch_cells

    def from_row(plane, step, shift):
        pairs = []
        for r in range(row_count):
            src = r + step
            if 0 <= src < row_count:
                for b in range(loop_size):
                    pairs.append((src * loop_size + (b + shift) % loop_size, r * loop_size + b))
        return lax.ppermute(plane, ("row", "circ"), pairs)

    def along_circ(value, shift):
        return lax.ppermute(
            value, "circ", [((b + shift) % loop_size, b) for b in range(loop_size)]
        )

    def picks(section_index):
        low_offset = offsets[section_index, lower_face]
        high_offset = (loop_cells - offsets[section_index, upper_face]) % loop_cells
        offs = jnp.stack([low_offset, high_offset])
        coarse = offs // pitch_cells
        fine = offs % pitch_cells
        sources = jnp.stack([lower_src, upper_src])
        dq = (coarse + passage_shift[sources] - passage_shift[row_id]) % loop_size
        first_col = jnp.arange(pitch_cells, dtype=jnp.int32)[None, :] + donor_step[0]
        weights = donor_weight[0]
        rows = jnp.arange(window, dtype=jnp.int32)[None, :, None]
        pick = jnp.where(rows == first_col[:, None, :], weights[:, None, :], 0.0) + jnp.where(
            rows == first_col[:, None, :] + 1, 1.0 - weights[:, None, :], 0.0
        )
        return dq, fine, pick.reshape(2, window // pitch_cells, pitch_cells, pitch_cells)

    def ghosts(last_plane, first_plane, section_index):
        dq, fine, pick = picks(section_index)
        first = RADICES[0]
        digit = dq % first
        blocks = []
        for d, (plane, step) in enumerate(((last_plane, -1), (first_plane, 1))):
            got = [from_row(plane, step, j) for j in range(first + 2)]
            span3 = jnp.concatenate(
                [lax.select_n(digit[d], *got[i : i + first]) for i in range(3)], axis=-1
            )
            cut = lax.dynamic_slice_in_dim(span3, fine[d], window, axis=-1)
            blocks.append(jnp.stack([cut[..., i * pitch_cells : (i + 1) * pitch_cells] for i in range(window // pitch_cells)]))
        stack = jnp.stack(blocks)
        span = first
        rest = dq // first
        for radix in RADICES[1:]:
            digit = rest % radix
            rest = rest // radix
            got = [stack] + [along_circ(stack, span * c) for c in range(1, radix)]
            stack = jnp.stack([lax.select_n(digit[d], *[g[d] for g in got]) for d in range(2)])
            span *= radix
        comps, radial = last_plane.shape[0], last_plane.shape[1]
        win = stack.reshape(2, window // pitch_cells, comps * radial, pitch_cells)
        out = [
            sum(
                jnp.dot(win[d, i], pick[d, i], precision=lax.Precision.HIGHEST)
                for i in range(window // pitch_cells)
            ).reshape(comps, radial, pitch_cells)
            for d in range(2)
        ]
        return out[0], out[1]

    def evaluate(fields, section_index):
        first_plane = fields[:, 0]
        last_plane = fields[:, -1]
        lower_ghost, upper_ghost = ghosts(last_plane, first_plane, section_index)
        lower_ghost = jnp.where(row_id == 0, first_plane, lower_ghost)
        upper_ghost = jnp.where(row_id == row_count - 1, last_plane, upper_ghost)
        around_ext = extended(fields, (("circ", 3),), 1)
        return combine(
            fields,
            axial_pad(fields, lower_ghost, upper_ghost),
            radial_pad(fields),
            around_ext,
            velocity,
        )

    section_one = flow_state + TIME_STEP * evaluate(flow_state, 0)
    section_two = 0.75 * flow_state + 0.25 * (section_one + TIME_STEP * evaluate(section_one, 1))
    return 1.0 / 3.0 * flow_state + 2.0 / 3.0 * (section_two + TIME_STEP * evaluate(section_two, 2))


def solution(mesh):
    placed = (
        P(None, "row", None, "circ"),
        P(None, "row", None, "circ"),
        P(),
        P(),
        P("row", None, "circ"),
        P("row", None, "circ"),
    )
    return jax.shard_map(
        local, mesh=mesh, in_specs=placed, out_specs=P(None, "row", None, "circ"), check_vma=False
    )
```

```python
import jax
import jax.numpy as jnp
from jax import lax
from jax.sharding import PartitionSpec as P

SMAG_COEF = 0.1
TIME_STEP = 0.25
RADICES = (8, 4)


def combine(fields, axial_ext, radial_ext, around_ext, velocity):
    d_axial = 0.5 * (axial_ext[:, 2:] - axial_ext[:, :-2])
    d_radial = 0.5 * (radial_ext[:, :, 2:] - radial_ext[:, :, :-2])
    d_around = 0.5 * (around_ext[..., 2:] - around_ext[..., :-2])
    laplace = (
        axial_ext[:, 2:]
        + axial_ext[:, :-2]
        + radial_ext[:, :, 2:]
        + radial_ext[:, :, :-2]
        + around_ext[..., 2:]
        + around_ext[..., :-2]
        - 6.0 * fields
    )
    strain = jnp.sum(d_axial[1:4] ** 2 + d_radial[1:4] ** 2 + d_around[1:4] ** 2, axis=0)
    eddy_visc = SMAG_COEF * jnp.sqrt(strain + 1.0)
    return eddy_visc * laplace - (
        velocity[0] * d_axial + velocity[1] * d_radial + velocity[2] * d_around
    )


def radial_pad(fields):
    return jnp.concatenate([fields[:, :, :1], fields, fields[:, :, -1:]], axis=2)


def axial_pad(fields, lower_ghost, upper_ghost):
    return jnp.concatenate([lower_ghost[:, None], fields, upper_ghost[:, None]], axis=1)


def local(flow_state, velocity, offsets, passage_shift, donor_step, donor_weight):
    row_count = lax.axis_size("row")
    loop_size = lax.axis_size("circ")
    row_id = lax.axis_index("row")
    pitch_cells = flow_state.shape[-1]
    planes = flow_state.shape[1]
    loop_cells = pitch_cells * loop_size
    comps, radial = flow_state.shape[0], flow_state.shape[2]
    window = 2 * pitch_cells
    lower_src = jnp.maximum(row_id - 1, 0)
    upper_src = jnp.minimum(row_id + 1, row_count - 1)
    lower_face = jnp.maximum(row_id - 1, 0)
    upper_face = jnp.minimum(row_id, row_count - 2)
    sources = jnp.stack([lower_src, upper_src])

    def along_row(value, step):
        return lax.ppermute(
            value, "row", [(r + step, r) for r in range(row_count) if 0 <= r + step < row_count]
        )

    def along_circ(value, shift):
        return lax.ppermute(
            value, "circ", [((b + shift) % loop_size, b) for b in range(loop_size)]
        )

    def circ_halo(cells):
        count = loop_size
        head = cells[..., :1]
        tail = cells[..., -1:]
        return jnp.concatenate(
            [
                lax.ppermute(tail, "circ", [(i, (i + 1) % count) for i in range(count)]),
                cells,
                lax.ppermute(head, "circ", [((i + 1) % count, i) for i in range(count)]),
            ],
            axis=-1,
        )

    def picks(section_index):
        low_offset = offsets[section_index, lower_face]
        high_offset = (loop_cells - offsets[section_index, upper_face]) % loop_cells
        offs = jnp.stack([low_offset, high_offset])
        coarse = offs // pitch_cells
        fine = offs % pitch_cells
        sources = jnp.stack([lower_src, upper_src])
        dq = (coarse + passage_shift[sources] - passage_shift[row_id]) % loop_size
        first_col = jnp.arange(pitch_cells, dtype=jnp.int32)[None, :] + donor_step[0]
        weights = donor_weight[0]
        rows = jnp.arange(window, dtype=jnp.int32)[None, :, None]
        pick = jnp.where(rows == first_col[:, None, :], weights[:, None, :], 0.0) + jnp.where(
            rows == first_col[:, None, :] + 1, 1.0 - weights[:, None, :], 0.0
        )
        return dq, fine, pick.reshape(2, window // pitch_cells, pitch_cells, pitch_cells)

    def ghosts(last_plane, first_plane, section_index, fields):
        dq, fine_col, pick = picks(section_index)
        faces = jnp.stack([along_row(last_plane, -1), along_row(first_plane, 1)])
        around = circ_halo(fields)
        faces, around = lax.optimization_barrier((faces, around))
        first = RADICES[0]
        got = [faces] + [along_circ(faces, j) for j in range(1, first + 2)]
        digit = dq % first
        blocks = []
        for d in range(2):
            span3 = jnp.concatenate(
                [lax.select_n(digit[d], *[g[d] for g in got[i : i + first]]) for i in range(3)], axis=-1
            )
            cut = lax.dynamic_slice_in_dim(span3, fine_col[d], window, axis=-1)
            blocks.append(
                jnp.stack([cut[..., i * pitch_cells : (i + 1) * pitch_cells] for i in range(window // pitch_cells)])
            )
        stack = jnp.stack(blocks)
        span = first
        rest = dq // first
        for radix in RADICES[1:]:
            digit = rest % radix
            rest = rest // radix
            got = [stack] + [along_circ(stack, span * c) for c in range(1, radix)]
            stack = jnp.stack([lax.select_n(digit[d], *[g[d] for g in got]) for d in range(2)])
            span *= radix
        win = stack.reshape(2, window // pitch_cells, comps * radial, pitch_cells)
        out = [
            sum(
                jnp.dot(win[d, i], pick[d, i], precision=lax.Precision.HIGHEST)
                for i in range(window // pitch_cells)
            ).reshape(comps, radial, pitch_cells)
            for d in range(2)
        ]
        lower = jnp.where(row_id == 0, first_plane, out[0])
        upper = jnp.where(row_id == row_count - 1, last_plane, out[1])
        return lower, upper, around

    def evaluate(fields, section_index):
        first_plane = fields[:, 0]
        last_plane = fields[:, -1]
        lower_ghost, upper_ghost, around_ext = ghosts(last_plane, first_plane, section_index, fields)
        return combine(
            fields,
            axial_pad(fields, lower_ghost, upper_ghost),
            radial_pad(fields),
            around_ext,
            velocity,
        )

    section_one = flow_state + TIME_STEP * evaluate(flow_state, 0)
    section_two = 0.75 * flow_state + 0.25 * (section_one + TIME_STEP * evaluate(section_one, 1))
    return 1.0 / 3.0 * flow_state + 2.0 / 3.0 * (section_two + TIME_STEP * evaluate(section_two, 2))


def solution(mesh):
    placed = (
        P(None, "row", None, "circ"),
        P(None, "row", None, "circ"),
        P(),
        P(),
        P("row", None, "circ"),
        P("row", None, "circ"),
    )
    return jax.shard_map(
        local, mesh=mesh, in_specs=placed, out_specs=P(None, "row", None, "circ"), check_vma=False
    )
```

```python
import jax
import jax.numpy as jnp
from jax import lax
from jax.sharding import PartitionSpec as P

SMAG_COEF = 0.1
TIME_STEP = 0.25
RADICES = (8, 4)


def combine(fields, axial_ext, radial_ext, halo, velocity):
    before = jnp.concatenate([halo[0], fields[..., :-1]], axis=-1)
    after = jnp.concatenate([fields[..., 1:], halo[1]], axis=-1)
    d_axial = 0.5 * (axial_ext[:, 2:] - axial_ext[:, :-2])
    d_radial = 0.5 * (radial_ext[:, :, 2:] - radial_ext[:, :, :-2])
    d_around = 0.5 * (after - before)
    laplace = (
        axial_ext[:, 2:]
        + axial_ext[:, :-2]
        + radial_ext[:, :, 2:]
        + radial_ext[:, :, :-2]
        + after
        + before
        - 6.0 * fields
    )
    strain = jnp.sum(d_axial[1:4] ** 2 + d_radial[1:4] ** 2 + d_around[1:4] ** 2, axis=0)
    eddy_visc = SMAG_COEF * jnp.sqrt(strain + 1.0)
    return eddy_visc * laplace - (
        velocity[0] * d_axial + velocity[1] * d_radial + velocity[2] * d_around
    )


def radial_pad(fields):
    return jnp.concatenate([fields[:, :, :1], fields, fields[:, :, -1:]], axis=2)


def axial_pad(fields, lower_ghost, upper_ghost):
    return jnp.concatenate([lower_ghost[:, None], fields, upper_ghost[:, None]], axis=1)


def local(flow_state, velocity, offsets, passage_shift, donor_step, donor_weight):
    row_count = lax.axis_size("row")
    loop_size = lax.axis_size("circ")
    row_id = lax.axis_index("row")
    pitch_cells = flow_state.shape[-1]
    planes = flow_state.shape[1]
    loop_cells = pitch_cells * loop_size
    comps, radial = flow_state.shape[0], flow_state.shape[2]
    window = 2 * pitch_cells
    lower_src = jnp.maximum(row_id - 1, 0)
    upper_src = jnp.minimum(row_id + 1, row_count - 1)
    lower_face = jnp.maximum(row_id - 1, 0)
    upper_face = jnp.minimum(row_id, row_count - 2)
    sources = jnp.stack([lower_src, upper_src])

    def along_row(value, step):
        return lax.ppermute(
            value, "row", [(r + step, r) for r in range(row_count) if 0 <= r + step < row_count]
        )

    def along_circ(value, shift):
        return lax.ppermute(
            value, "circ", [((b + shift) % loop_size, b) for b in range(loop_size)]
        )

    def circ_halo(cells):
        count = loop_size
        head = cells[..., :1]
        tail = cells[..., -1:]
        return (
            lax.ppermute(tail, "circ", [(i, (i + 1) % count) for i in range(count)]),
            lax.ppermute(head, "circ", [((i + 1) % count, i) for i in range(count)]),
        )

    def picks(section_index):
        low_offset = offsets[section_index, lower_face]
        high_offset = (loop_cells - offsets[section_index, upper_face]) % loop_cells
        offs = jnp.stack([low_offset, high_offset])
        coarse = offs // pitch_cells
        fine = offs % pitch_cells
        sources = jnp.stack([lower_src, upper_src])
        dq = (coarse + passage_shift[sources] - passage_shift[row_id]) % loop_size
        first_col = jnp.arange(pitch_cells, dtype=jnp.int32)[None, :] + donor_step[0]
        weights = donor_weight[0]
        rows = jnp.arange(window, dtype=jnp.int32)[None, :, None]
        pick = jnp.where(rows == first_col[:, None, :], weights[:, None, :], 0.0) + jnp.where(
            rows == first_col[:, None, :] + 1, 1.0 - weights[:, None, :], 0.0
        )
        return dq, fine, pick.reshape(2, window // pitch_cells, pitch_cells, pitch_cells)

    def ghosts(last_plane, first_plane, section_index, fields):
        dq, fine_col, pick = picks(section_index)
        faces = jnp.stack([along_row(last_plane, -1), along_row(first_plane, 1)])
        around = circ_halo(fields)
        faces, around = lax.optimization_barrier((faces, around))
        first = RADICES[0]
        got = [faces] + [along_circ(faces, j) for j in range(1, first + 2)]
        digit = dq % first
        blocks = []
        for d in range(2):
            span3 = jnp.concatenate(
                [lax.select_n(digit[d], *[g[d] for g in got[i : i + first]]) for i in range(3)], axis=-1
            )
            cut = lax.dynamic_slice_in_dim(span3, fine_col[d], window, axis=-1)
            blocks.append(
                jnp.stack([cut[..., i * pitch_cells : (i + 1) * pitch_cells] for i in range(window // pitch_cells)])
            )
        stack = jnp.stack(blocks)
        span = first
        rest = dq // first
        for radix in RADICES[1:]:
            digit = rest % radix
            rest = rest // radix
            got = [stack] + [along_circ(stack, span * c) for c in range(1, radix)]
            stack = jnp.stack([lax.select_n(digit[d], *[g[d] for g in got]) for d in range(2)])
            span *= radix
        win = stack.reshape(2, window // pitch_cells, comps * radial, pitch_cells)
        out = [
            sum(
                jnp.dot(win[d, i], pick[d, i], precision=lax.Precision.HIGHEST)
                for i in range(window // pitch_cells)
            ).reshape(comps, radial, pitch_cells)
            for d in range(2)
        ]
        lower = jnp.where(row_id == 0, first_plane, out[0])
        upper = jnp.where(row_id == row_count - 1, last_plane, out[1])
        return lower, upper, around

    def evaluate(fields, section_index):
        first_plane = fields[:, 0]
        last_plane = fields[:, -1]
        lower_ghost, upper_ghost, around_ext = ghosts(last_plane, first_plane, section_index, fields)
        return combine(
            fields,
            axial_pad(fields, lower_ghost, upper_ghost),
            radial_pad(fields),
            around_ext,
            velocity,
        )

    section_one = flow_state + TIME_STEP * evaluate(flow_state, 0)
    section_two = 0.75 * flow_state + 0.25 * (section_one + TIME_STEP * evaluate(section_one, 1))
    return 1.0 / 3.0 * flow_state + 2.0 / 3.0 * (section_two + TIME_STEP * evaluate(section_two, 2))


def solution(mesh):
    placed = (
        P(None, "row", None, "circ"),
        P(None, "row", None, "circ"),
        P(),
        P(),
        P("row", None, "circ"),
        P("row", None, "circ"),
    )
    return jax.shard_map(
        local, mesh=mesh, in_specs=placed, out_specs=P(None, "row", None, "circ"), check_vma=False
    )
```

```python
import jax
import jax.numpy as jnp
from jax import lax
from jax.sharding import PartitionSpec as P

SMAG_COEF = 0.1
TIME_STEP = 0.25
RADICES = (4, 8)


def combine(fields, axial_ext, radial_ext, around_ext, velocity):
    d_axial = 0.5 * (axial_ext[:, 2:] - axial_ext[:, :-2])
    d_radial = 0.5 * (radial_ext[:, :, 2:] - radial_ext[:, :, :-2])
    d_around = 0.5 * (around_ext[..., 2:] - around_ext[..., :-2])
    laplace = (
        axial_ext[:, 2:]
        + axial_ext[:, :-2]
        + radial_ext[:, :, 2:]
        + radial_ext[:, :, :-2]
        + around_ext[..., 2:]
        + around_ext[..., :-2]
        - 6.0 * fields
    )
    strain = jnp.sum(d_axial[1:4] ** 2 + d_radial[1:4] ** 2 + d_around[1:4] ** 2, axis=0)
    eddy_visc = SMAG_COEF * jnp.sqrt(strain + 1.0)
    return eddy_visc * laplace - (
        velocity[0] * d_axial + velocity[1] * d_radial + velocity[2] * d_around
    )


def radial_pad(fields):
    return jnp.concatenate([fields[:, :, :1], fields, fields[:, :, -1:]], axis=2)


def axial_pad(fields, lower_ghost, upper_ghost):
    return jnp.concatenate([lower_ghost[:, None], fields, upper_ghost[:, None]], axis=1)


def local(flow_state, velocity, offsets, passage_shift, donor_step, donor_weight):
    row_count = lax.axis_size("row")
    loop_size = lax.axis_size("circ")
    row_id = lax.axis_index("row")
    pitch_cells = flow_state.shape[-1]
    planes = flow_state.shape[1]
    loop_cells = pitch_cells * loop_size
    comps, radial = flow_state.shape[0], flow_state.shape[2]
    window = 2 * pitch_cells
    lower_src = jnp.maximum(row_id - 1, 0)
    upper_src = jnp.minimum(row_id + 1, row_count - 1)
    lower_face = jnp.maximum(row_id - 1, 0)
    upper_face = jnp.minimum(row_id, row_count - 2)
    sources = jnp.stack([lower_src, upper_src])

    def along_row(value, step):
        return lax.ppermute(
            value, "row", [(r + step, r) for r in range(row_count) if 0 <= r + step < row_count]
        )

    def along_circ(value, shift):
        return lax.ppermute(
            value, "circ", [((b + shift) % loop_size, b) for b in range(loop_size)]
        )

    def circ_halo(cells):
        count = loop_size
        head = cells[..., :1]
        tail = cells[..., -1:]
        return jnp.concatenate(
            [
                lax.ppermute(tail, "circ", [(i, (i + 1) % count) for i in range(count)]),
                cells,
                lax.ppermute(head, "circ", [((i + 1) % count, i) for i in range(count)]),
            ],
            axis=-1,
        )

    def picks(section_index):
        low_offset = offsets[section_index, lower_face]
        high_offset = (loop_cells - offsets[section_index, upper_face]) % loop_cells
        offs = jnp.stack([low_offset, high_offset])
        coarse = offs // pitch_cells
        fine = offs % pitch_cells
        sources = jnp.stack([lower_src, upper_src])
        dq = (coarse + passage_shift[sources] - passage_shift[row_id]) % loop_size
        first_col = jnp.arange(pitch_cells, dtype=jnp.int32)[None, :] + donor_step[0]
        weights = donor_weight[0]
        rows = jnp.arange(window, dtype=jnp.int32)[None, :, None]
        pick = jnp.where(rows == first_col[:, None, :], weights[:, None, :], 0.0) + jnp.where(
            rows == first_col[:, None, :] + 1, 1.0 - weights[:, None, :], 0.0
        )
        return dq, fine, pick.reshape(2, window // pitch_cells, pitch_cells, pitch_cells)

    def ghosts(last_plane, first_plane, section_index, fields):
        dq, fine_col, pick = picks(section_index)
        faces = jnp.stack([along_row(last_plane, -1), along_row(first_plane, 1)])
        around = circ_halo(fields)
        faces, around = lax.optimization_barrier((faces, around))
        first = RADICES[0]
        got = [faces] + [along_circ(faces, j) for j in range(1, first + 2)]
        digit = dq % first
        blocks = []
        for d in range(2):
            span3 = jnp.concatenate(
                [lax.select_n(digit[d], *[g[d] for g in got[i : i + first]]) for i in range(3)], axis=-1
            )
            cut = lax.dynamic_slice_in_dim(span3, fine_col[d], window, axis=-1)
            blocks.append(
                jnp.stack([cut[..., i * pitch_cells : (i + 1) * pitch_cells] for i in range(window // pitch_cells)])
            )
        stack = jnp.stack(blocks)
        span = first
        rest = dq // first
        for radix in RADICES[1:]:
            digit = rest % radix
            rest = rest // radix
            got = [stack] + [along_circ(stack, span * c) for c in range(1, radix)]
            stack = jnp.stack([lax.select_n(digit[d], *[g[d] for g in got]) for d in range(2)])
            span *= radix
        win = stack.reshape(2, window // pitch_cells, comps * radial, pitch_cells)
        out = [
            sum(
                jnp.dot(win[d, i], pick[d, i], precision=lax.Precision.HIGHEST)
                for i in range(window // pitch_cells)
            ).reshape(comps, radial, pitch_cells)
            for d in range(2)
        ]
        lower = jnp.where(row_id == 0, first_plane, out[0])
        upper = jnp.where(row_id == row_count - 1, last_plane, out[1])
        return lower, upper, around

    def evaluate(fields, section_index):
        first_plane = fields[:, 0]
        last_plane = fields[:, -1]
        lower_ghost, upper_ghost, around_ext = ghosts(last_plane, first_plane, section_index, fields)
        return combine(
            fields,
            axial_pad(fields, lower_ghost, upper_ghost),
            radial_pad(fields),
            around_ext,
            velocity,
        )

    section_one = flow_state + TIME_STEP * evaluate(flow_state, 0)
    section_two = 0.75 * flow_state + 0.25 * (section_one + TIME_STEP * evaluate(section_one, 1))
    return 1.0 / 3.0 * flow_state + 2.0 / 3.0 * (section_two + TIME_STEP * evaluate(section_two, 2))


def solution(mesh):
    placed = (
        P(None, "row", None, "circ"),
        P(None, "row", None, "circ"),
        P(),
        P(),
        P("row", None, "circ"),
        P("row", None, "circ"),
    )
    return jax.shard_map(
        local, mesh=mesh, in_specs=placed, out_specs=P(None, "row", None, "circ"), check_vma=False
    )
```

```python
import jax
import jax.numpy as jnp
from jax import lax
from jax.sharding import PartitionSpec as P


SMAG_COEF = 0.1
TIME_STEP = 0.25
RADICES = (8, 4)


def combine(fields, axial_ext, radial_ext, around_ext, velocity):
    d_axial = 0.5 * (axial_ext[:, 2:] - axial_ext[:, :-2])
    d_radial = 0.5 * (radial_ext[:, :, 2:] - radial_ext[:, :, :-2])
    d_around = 0.5 * (around_ext[..., 2:] - around_ext[..., :-2])
    laplace = (
        axial_ext[:, 2:]
        + axial_ext[:, :-2]
        + radial_ext[:, :, 2:]
        + radial_ext[:, :, :-2]
        + around_ext[..., 2:]
        + around_ext[..., :-2]
        - 6.0 * fields
    )
    strain = jnp.sum(d_axial[1:4] ** 2 + d_radial[1:4] ** 2 + d_around[1:4] ** 2, axis=0)
    eddy_visc = SMAG_COEF * jnp.sqrt(strain + 1.0)
    return eddy_visc * laplace - (
        velocity[0] * d_axial + velocity[1] * d_radial + velocity[2] * d_around
    )


def radial_pad(fields):
    return jnp.concatenate([fields[:, :, :1], fields, fields[:, :, -1:]], axis=2)


def axial_pad(fields, lower_ghost, upper_ghost):
    return jnp.concatenate([lower_ghost[:, None], fields, upper_ghost[:, None]], axis=1)


def local(flow_state, velocity, offsets, passage_shift, donor_step, donor_weight):
    row_count = lax.axis_size("row")
    loop_size = lax.axis_size("circ")
    row_id = lax.axis_index("row")
    pitch_cells = flow_state.shape[-1]
    loop_cells = pitch_cells * loop_size
    comps, radial = flow_state.shape[0], flow_state.shape[2]
    window = 2 * pitch_cells
    lower_src = jnp.maximum(row_id - 1, 0)
    upper_src = jnp.minimum(row_id + 1, row_count - 1)
    lower_face = jnp.maximum(row_id - 1, 0)
    upper_face = jnp.minimum(row_id, row_count - 2)
    sources = jnp.stack([lower_src, upper_src])

    def along_row(value, step):
        return lax.ppermute(
            value, "row", [(r + step, r) for r in range(row_count) if 0 <= r + step < row_count]
        )

    def along_circ(value, shift):
        return lax.ppermute(
            value, "circ", [((b + shift) % loop_size, b) for b in range(loop_size)]
        )

    def circ_halo(cells):
        count = loop_size
        head = cells[..., :1]
        tail = cells[..., -1:]
        return jnp.concatenate(
            [
                lax.ppermute(tail, "circ", [(i, (i + 1) % count) for i in range(count)]),
                cells,
                lax.ppermute(head, "circ", [((i + 1) % count, i) for i in range(count)]),
            ],
            axis=-1,
        )

    def picks(section_index):
        low_offset = offsets[section_index, lower_face]
        high_offset = (loop_cells - offsets[section_index, upper_face]) % loop_cells
        offs = jnp.stack([low_offset, high_offset])
        coarse = offs // pitch_cells
        fine = offs % pitch_cells
        sources = jnp.stack([lower_src, upper_src])
        dq = (coarse + passage_shift[sources] - passage_shift[row_id]) % loop_size
        first_col = jnp.arange(pitch_cells, dtype=jnp.int32)[None, :] + donor_step[0]
        weights = donor_weight[0]
        rows = jnp.arange(window, dtype=jnp.int32)[None, :, None]
        pick = jnp.where(rows == first_col[:, None, :], weights[:, None, :], 0.0) + jnp.where(
            rows == first_col[:, None, :] + 1, 1.0 - weights[:, None, :], 0.0
        )
        return dq, fine, pick.reshape(2, window // pitch_cells, pitch_cells, pitch_cells)

    def ghosts(last_plane, first_plane, section_index, fields):
        dq, fine_col, pick = picks(section_index)
        faces = jnp.stack([along_row(last_plane, -1), along_row(first_plane, 1)])
        around = circ_halo(fields)
        first = RADICES[0]
        got = [faces] + [along_circ(faces, j) for j in range(1, first + 2)]
        digit = dq % first
        blocks = []
        for d in range(2):
            span3 = jnp.concatenate(
                [lax.select_n(digit[d], *[g[d] for g in got[i : i + first]]) for i in range(3)], axis=-1
            )
            cut = lax.dynamic_slice_in_dim(span3, fine_col[d], window, axis=-1)
            blocks.append(
                jnp.stack([cut[..., i * pitch_cells : (i + 1) * pitch_cells] for i in range(window // pitch_cells)])
            )
        stack = jnp.stack(blocks)
        span = first
        rest = dq // first
        for radix in RADICES[1:]:
            digit = rest % radix
            rest = rest // radix
            got = [stack] + [along_circ(stack, span * c) for c in range(1, radix)]
            stack = jnp.stack([lax.select_n(digit[d], *[g[d] for g in got]) for d in range(2)])
            span *= radix
        win = stack.reshape(2, window // pitch_cells, comps * radial, pitch_cells)
        out = [
            sum(
                jnp.dot(win[d, i], pick[d, i], precision=lax.Precision.HIGHEST)
                for i in range(window // pitch_cells)
            ).reshape(comps, radial, pitch_cells)
            for d in range(2)
        ]
        lower = jnp.where(row_id == 0, first_plane, out[0])
        upper = jnp.where(row_id == row_count - 1, last_plane, out[1])
        return lower, upper, around

    def evaluate_section(fields, section_index):
        first_plane = fields[:, 0]
        last_plane = fields[:, -1]
        lower_ghost, upper_ghost, around_ext = ghosts(last_plane, first_plane, section_index, fields)
        return combine(
            fields,
            axial_pad(fields, lower_ghost, upper_ghost),
            radial_pad(fields),
            around_ext,
            velocity,
        )

    section_one = flow_state + TIME_STEP * evaluate_section(flow_state, 0)
    section_two = 0.75 * flow_state + 0.25 * (section_one + TIME_STEP * evaluate_section(section_one, 1))
    return 1.0 / 3.0 * flow_state + 2.0 / 3.0 * (section_two + TIME_STEP * evaluate_section(section_two, 2))


def solution(mesh):
    placed = (
        P(None, "row", None, "circ"),
        P(None, "row", None, "circ"),
        P(),
        P(),
        P("row", None, "circ"),
        P("row", None, "circ"),
    )
    return jax.shard_map(
        local, mesh=mesh, in_specs=placed, out_specs=P(None, "row", None, "circ"), check_vma=False
    )
```
